128 devices in a mesh: band: 4 (over z), sector: 32 (over y, x, core).
Axes of the slice: x: 4, y: 4, z: 4, core: 2. Of those that a mesh axis runs over, the one named last changes fastest.
Arguments:
- control: float32 [762, 64, 4096], P(None, 'band', 'sector'), may hold values from -16 to 16
- direction: float32 [762, 64, 4096], P(None, 'band', 'sector'), may hold values from -16 to 16
- step_lengths: float32 [4], replicated, may hold values from 0.25 to 2
- level_root: bfloat16 [762, 762], replicated, may hold values from -0.21875 to 0.21875
- lon_decay: float32 [762], replicated, as said below
- lat_decay: float32 [762], replicated, as said below
- obs_operator: bfloat16 [128, 762], replicated, may hold values from -0.21875 to 0.21875
- obs_values: float32 [131072, 128], P(('band', 'sector')), may hold values from -6 to 6
- obs_inv_err: float32 [131072, 128], P(('band', 'sector')), may hold values from 0.5 to 2
- obs_cols: int32 [131072], P(('band', 'sector')), may hold values from 0 to 1918, as said below
- obs_weights: float32 [131072, 4], P(('band', 'sector')), may hold values from 0.1 to 1
- counts: int32 [128, 128], P(('band', 'sector')), may hold values from 1 to 8, as said below
Outputs:
- departures: float32 [131072, 4, 128], P(('band', 'sector'))
- costs: float32 [4], replicated
The draws below stay inside these ranges and needn't reach their ends.
Inputs may be any that keep to these rules, and one draw needn't show every extreme that they name: `lon_decay`: every line's coefficient lies strictly between 0 and 1. `lat_decay`: every line's coefficient lies strictly between 0 and 1. `obs_cols`: a column lat * 128 + lon of the owner's block with lat <= 14 and lon <= 126; unused slots hold such columns too. `counts`: in every draw some owner receives 8 rows from every device, and some device fills all its slots to every owner.
All inputs are finite; a program needn't handle non-finite values.
Results may differ from the reference program's by a relative error of at most 0.0039.
Values sent between devices are 32-bit elements; how exact they have to be, the bound alone decides.
No kernel may reach another device: no remote copies, remote signals or barrier semaphores. Data moves between devices by JAX's collectives and lax.ppermute only.
A program may use at most 256 MiB of HBM per device.

```python
import math
import jax
import jax.numpy as jnp
from jax import lax

NV = 6
LEV = 127
CHAN = 128
TRIALS = 4
LAT_DEV = 16
LON_DEV = 128
CAP = 8
LINES = 762
NLAT = 64
NLON = 4096
OBS = 131072
DEVICES = 128


def draw_rates(key, length, chain_length):
    ranking = jax.random.permutation(jax.random.fold_in(key, 1), length)
    slow_count = length // 2
    slow_lines = ranking < slow_count
    keeping = jax.random.uniform(jax.random.fold_in(key, 2), (length,), jnp.float32, 0.2, 1.5)
    memory = jax.random.uniform(jax.random.fold_in(key, 3), (length,), jnp.float32, 30.0, 50.0)
    return jnp.where(slow_lines, jnp.exp(-keeping / chain_length), jnp.exp(-1.0 / memory)).astype(jnp.float32)


def draw_field(key):
    lines_total = NV * LEV
    line_part = jax.random.uniform(jax.random.fold_in(key, 1), (lines_total,), jnp.float32, -0.5, 0.5)
    lat_part = jnp.arange(NLAT).astype(jnp.float32) / (NLAT - 1) - 0.5
    lon_part = jnp.arange(NLON).astype(jnp.float32) / (NLON - 1) - 0.5
    noise = jnp.clip(jax.random.normal(jax.random.fold_in(key, 2), (lines_total, NLAT, NLON), jnp.float32), -3.5, 3.5)
    lat_gain = math.log(3.0)
    lon_gain = math.log(1.5)
    exponent = math.log(10.0) * line_part[:, None, None] + lat_gain * lat_part[None, :, None] + lon_gain * lon_part[None, None, :]
    return (noise * jnp.exp(0.5 * exponent)).astype(jnp.float32)


def draw_control(key, part):
    return draw_field(jax.random.fold_in(key, 41))


def draw_direction(key, part):
    return draw_field(jax.random.fold_in(key, 42))


def draw_lon_decay(key, part):
    return draw_rates(jax.random.fold_in(key, 11), NV * LEV, NLON)


def draw_lat_decay(key, part):
    return draw_rates(jax.random.fold_in(key, 12), NV * LEV, NLAT)


def draw_counts(key, part):
    base_key = jax.random.fold_in(key, 21)
    filled = jax.random.randint(jax.random.fold_in(base_key, 1), (DEVICES, DEVICES), 1, CAP + 1)
    full_target = jax.random.randint(jax.random.fold_in(base_key, 2), (), 0, DEVICES)
    full_sender = jax.random.randint(jax.random.fold_in(base_key, 3), (), 0, DEVICES)
    index_grid = jnp.arange(DEVICES)
    filled = jnp.where(index_grid[None, :] == full_target, CAP, filled)
    filled = jnp.where(index_grid[:, None] == full_sender, CAP, filled)
    return filled.astype(jnp.int32)


def draw_obs_cols(key, part):
    base_key = jax.random.fold_in(key, 31)
    lat_pick = jax.random.randint(jax.random.fold_in(base_key, 1), (OBS,), 0, LAT_DEV - 1)
    lon_pick = jax.random.randint(jax.random.fold_in(base_key, 2), (OBS,), 0, LON_DEV - 1)
    chosen = lat_pick * LON_DEV + lon_pick
    chosen = chosen.at[0].set((LAT_DEV - 2) * LON_DEV + LON_DEV - 2)
    return chosen.astype(jnp.int32)


def steps_of(key, shape, cuts, low, top_value):
    def one(axis_at, parts):
        heights = jax.random.uniform(jax.random.fold_in(jax.random.fold_in(key, 6), axis_at), (parts,), jnp.float32, low / len(cuts), top_value / len(cuts))
        return jnp.repeat(jnp.exp(heights), shape[axis_at] // parts).reshape((-1,) + (1,) * (len(shape) - axis_at - 1))

    loudness = one(*cuts[0])
    for cut in cuts[1:]:
        loudness = loudness * one(*cut)
    return loudness


def gaussian(own_key, shape, scale, bound, pieces=(), held_as=jnp.bfloat16):
    drawn = jax.random.normal(own_key, shape, jnp.float32) * scale
    if len(pieces) > 0:
        drawn = steps_of(own_key, shape, pieces, -0.22, 0.18) * drawn
    return jnp.clip(drawn, min=-bound, max=bound).astype(held_as)


def setup_inputs(seed: int = 0) -> dict:
    key_list = jax.random.split(jax.random.key(seed), 13)
    return {
        "control": draw_control(jax.random.fold_in(key_list[12], 71), 0),
        "direction": draw_direction(jax.random.fold_in(key_list[12], 71), 0),
        "step_lengths": jnp.clip(jax.random.uniform(key_list[2], (TRIALS,), jnp.float32, 0.25, 2.0), 0.25, 2.0),
        "level_root": gaussian(key_list[3], (LINES, LINES), LINES ** -0.5, 0.21875),
        "lon_decay": draw_lon_decay(jax.random.fold_in(key_list[12], 71), 0),
        "lat_decay": draw_lat_decay(jax.random.fold_in(key_list[12], 71), 0),
        "obs_operator": gaussian(key_list[6], (CHAN, LINES), LINES ** -0.5, 0.21875),
        "obs_values": gaussian(key_list[7], (OBS, CHAN), 1.0, 6.0, ((0, 128),), jnp.float32),
        "obs_inv_err": jnp.clip(jnp.exp(math.log(2.0) - 1.3862944 * jax.random.uniform(key_list[8], (OBS, CHAN), jnp.float32) ** steps_of(key_list[8], (OBS, CHAN), ((0, 128),), -0.2, 0.2)), 0.5, 2.0),
        "obs_cols": draw_obs_cols(jax.random.fold_in(key_list[12], 71), 0),
        "obs_weights": jnp.clip(0.1 + 0.9 * jax.random.uniform(key_list[10], (OBS, 4), jnp.float32) ** steps_of(key_list[10], (OBS, 4), ((0, 128),), -0.2, 0.2), 0.1, 1.0),
        "counts": draw_counts(jax.random.fold_in(key_list[12], 71), 0),
    }


def along_longitude(source, coefficient):

    def advance(carried, column):
        carried = coefficient[:, None] * carried + column
        return (carried, carried)
    final_state, filtered = lax.scan(advance, jnp.zeros(source.shape[:2], source.dtype), jnp.moveaxis(source, 2, 0))
    filtered = jnp.moveaxis(filtered, 0, 2)
    wrapped = final_state / (1.0 - coefficient ** NLON)[:, None]
    exponents = jnp.arange(1, NLON + 1).astype(source.dtype)
    powers = coefficient[:, None] ** exponents[None, :]
    filtered = filtered + powers[:, None, :] * wrapped[:, :, None]
    return filtered * jnp.sqrt(1.0 - coefficient * coefficient)[:, None, None]

def along_latitude(source, coefficient):

    def advance(carried, layer):
        carried = coefficient[:, None] * carried + layer
        return (carried, carried)
    final_state, filtered = lax.scan(advance, jnp.zeros((source.shape[0], source.shape[2]), source.dtype), jnp.moveaxis(source, 1, 0))
    filtered = jnp.moveaxis(filtered, 0, 1)
    return filtered * jnp.sqrt(1.0 - coefficient * coefficient)[:, None, None]

def reference(control, direction, step_lengths, level_root, lon_decay, lat_decay, obs_operator, obs_values, obs_inv_err, obs_cols, obs_weights, counts):
    control_lines = NV * LEV
    slot_index = jnp.arange(CAP).astype(jnp.int32)
    live_slot = (counts[:, :, None] > slot_index[None, None, :]).reshape(OBS)
    owner_device = jnp.arange(OBS).astype(jnp.int32) // CAP % DEVICES
    sector_count = NLON // LON_DEV
    row_lat = owner_device // sector_count * LAT_DEV + obs_cols // LON_DEV
    row_lon = owner_device % sector_count * LON_DEV + obs_cols % LON_DEV

    def one_trial(step_size):
        trial_field = control + step_size * direction
        background = jnp.sum(trial_field * trial_field)
        rounded = trial_field.astype(jnp.bfloat16)
        mixed_field = jnp.dot(level_root, rounded.reshape(control_lines, NLAT * NLON), preferred_element_type=jnp.float32)
        mixed_field = mixed_field.reshape(control_lines, NLAT, NLON)
        increment = along_latitude(along_longitude(mixed_field, lon_decay), lat_decay)
        profile = obs_weights[:, 0] * increment[:, row_lat, row_lon]
        profile = profile + obs_weights[:, 1] * increment[:, row_lat, row_lon + 1]
        profile = profile + obs_weights[:, 2] * increment[:, row_lat + 1, row_lon]
        profile = profile + obs_weights[:, 3] * increment[:, row_lat + 1, row_lon + 1]
        evolved = jnp.dot(obs_operator, profile.astype(jnp.bfloat16), preferred_element_type=jnp.float32)
        weighted = (evolved.T - obs_values) * obs_inv_err
        departures = jnp.where(live_slot[:, None], weighted, jnp.zeros_like(weighted))
        return (departures, background, jnp.sum(departures * departures))
    departures, background, misfit = lax.map(one_trial, step_lengths)
    cost_values = 0.5 * (background + misfit) / (control_lines * NLAT * NLON)
    return (jnp.transpose(departures, (1, 0, 2)), cost_values)
```

```python
import functools

import jax
import jax.numpy as jnp
from jax import lax
from jax.experimental import pallas as pl
from jax.experimental.pallas import tpu as pltpu
from jax.sharding import PartitionSpec as P

LANES = 128
SCAN_STEPS = 7
LINE_TILE = 256


def padded_lines(n):
    return -(-n // LINE_TILE) * LINE_TILE


def local_filter_kernel(lat_groups, mix_ref, x_ref, apow_ref, lat_ref, out_ref, end_ref):
    tile = mix_ref.shape[0]
    lane = lax.broadcasted_iota(jnp.int32, (tile, LANES), 1)
    decay = lat_ref[...]
    weights = mix_ref[...]
    state = None
    ends = jnp.zeros((tile, LANES), jnp.float32)
    for g in range(lat_groups):
        cols = pl.ds(g * LANES, LANES)
        v = jnp.dot(weights, x_ref[0, :, cols], preferred_element_type=jnp.float32)
        for s in range(SCAN_STEPS):
            shift = 1 << s
            moved = pltpu.roll(v, shift, 1)
            v = v + jnp.where(lane >= shift, apow_ref[s] * moved, 0.0)
        last = jnp.sum(jnp.where(lane == LANES - 1, v, 0.0), axis=1, keepdims=True)
        ends = jnp.where(lane == g, last, ends)
        state = v if state is None else decay * state + v
        out_ref[0, :, cols] = state
    end_ref[0] = ends


def local_filter(mix, xb, apow, lat_b):
    trials, kpad, cols = xb.shape
    groups = cols // LANES
    tiles = kpad // LINE_TILE
    flops = 2 * kpad * kpad * cols * trials + 30 * trials * kpad * cols
    bytes_accessed = xb.size * 2 + trials * kpad * cols * 4 + mix.size * 2 * trials
    return pl.pallas_call(
        functools.partial(local_filter_kernel, groups),
        grid=(trials, tiles),
        in_specs=[
            pl.BlockSpec((LINE_TILE, kpad), lambda t, k: (k, 0)),
            pl.BlockSpec((1, kpad, cols), lambda t, k: (t, 0, 0)),
            pl.BlockSpec((SCAN_STEPS, LINE_TILE, LANES), lambda t, k: (0, k, 0)),
            pl.BlockSpec((LINE_TILE, LANES), lambda t, k: (k, 0)),
        ],
        out_specs=[
            pl.BlockSpec((1, LINE_TILE, cols), lambda t, k: (t, k, 0)),
            pl.BlockSpec((1, LINE_TILE, LANES), lambda t, k: (t, k, 0)),
        ],
        out_shape=[
            jax.ShapeDtypeStruct((trials, kpad, cols), jnp.float32),
            jax.ShapeDtypeStruct((trials, kpad, LANES), jnp.float32),
        ],
        compiler_params=pltpu.CompilerParams(dimension_semantics=("arbitrary", "arbitrary")),
        cost_estimate=pl.CostEstimate(
            flops=flops, bytes_accessed=bytes_accessed, transcendentals=0
        ),
    )(mix, xb, apow, lat_b)


def shifted(x, axis, shift):
    n = lax.axis_size(axis)
    return lax.ppermute(x, axis, [(s, (s + shift) % n) for s in range(n)])


def xor_total(x, axes):
    for axis in axes:
        n = lax.axis_size(axis)
        bit = 1
        while bit < n:
            x = x + lax.ppermute(x, axis, [(s, s ^ bit) for s in range(n)])
            bit *= 2
    return x


def body(
    control,
    direction,
    step_lengths,
    level_root,
    lon_decay,
    lat_decay,
    obs_operator,
    obs_values,
    obs_inv_err,
    obs_cols,
    obs_weights,
    counts,
):
    num_lines, lat_dev, lon_dev = control.shape
    trials = step_lengths.shape[0]
    channels = obs_values.shape[1]
    bands = lax.axis_size("band")
    sectors = lax.axis_size("sector")
    devices_all = bands * sectors
    capacity = obs_cols.shape[0] // devices_all
    kpad = padded_lines(num_lines)
    extra = kpad - num_lines
    f32 = jnp.float32

    packed = jnp.concatenate(
        [obs_cols.astype(f32)[:, None], obs_weights], axis=1
    ).reshape(devices_all, capacity, 5)
    packed = lax.all_to_all(packed, ("band", "sector"), 0, 0, tiled=True)

    trial_fields = control[None] + step_lengths[:, None, None, None] * direction[None]
    background = jnp.sum(trial_fields * trial_fields, axis=(1, 2, 3))
    xb = trial_fields.astype(jnp.bfloat16).reshape(trials, num_lines, lat_dev * lon_dev)
    xb = jnp.pad(xb, ((0, 0), (0, extra), (0, 0)))
    mix = jnp.pad(level_root, ((0, extra), (0, extra)))

    a = jnp.pad(lon_decay, (0, extra), constant_values=0.5)
    b = jnp.pad(lat_decay, (0, extra), constant_values=0.5)
    log_a = jnp.log(a)
    log_b = jnp.log(b)
    spans = (2.0 ** jnp.arange(SCAN_STEPS)).astype(f32)
    apow = jnp.exp(spans[:, None] * log_a[None, :])
    apow = jnp.broadcast_to(apow[:, :, None], (SCAN_STEPS, kpad, LANES))
    lat_b = jnp.broadcast_to(b[:, None], (kpad, LANES))

    local, ends = local_filter(mix, xb, apow, lat_b)
    local = local.reshape(trials, kpad, lat_dev, lon_dev)
    lon_ends = ends[:, :, :lat_dev]

    sector_gain = jnp.exp(log_a * lon_dev)
    carried = shifted(lon_ends, "sector", 1)
    carried = carried + sector_gain[None, :, None] * shifted(lon_ends, "sector", 2)
    span = 2
    while span < sectors:
        gain = jnp.exp(log_a * (lon_dev * span))
        carried = carried + gain[None, :, None] * shifted(carried, "sector", span)
        span *= 2
    loop_gain = 1.0 - jnp.exp(log_a * (lon_dev * sectors))
    incoming = carried / loop_gain[None, :, None]

    rows = []
    state = jnp.zeros((trials, kpad), f32)
    for i in range(lat_dev):
        state = b[None, :] * state + incoming[:, :, i]
        rows.append(state)
    incoming_lat = jnp.stack(rows, axis=2)
    lon_rise = jnp.exp(log_a[:, None] * jnp.arange(1, lon_dev + 1).astype(f32)[None, :])
    lat_rise = jnp.exp(log_b[:, None] * jnp.arange(1, lat_dev + 1).astype(f32)[None, :])
    scale_a = jnp.sqrt(1.0 - a * a)
    scale_b = jnp.sqrt(1.0 - b * b)

    band_end = scale_a[None, :, None] * (
        local[:, :, lat_dev - 1, :] + lon_rise[None] * incoming_lat[:, :, lat_dev - 1, None]
    )
    band_ends = lax.all_gather(band_end, "band")
    me = lax.axis_index("band")
    source = jnp.arange(bands)
    power = (me - 1 - source).astype(f32)
    band_weight = jnp.where(
        (source < me)[:, None], jnp.exp(log_b[None, :] * (lat_dev * power)[:, None]), 0.0
    )
    entering = jnp.sum(band_weight[:, None, :, None] * band_ends, axis=0)

    increment = scale_b[None, :, None, None] * (
        scale_a[None, :, None, None]
        * (local + lon_rise[None, :, None, :] * incoming_lat[:, :, :, None])
        + lat_rise[None, :, :, None] * entering[:, :, None, :]
    )
    table = jnp.transpose(increment, (2, 3, 0, 1)).reshape(lat_dev * lon_dev, trials * kpad)

    where = packed[:, :, 0].astype(jnp.int32).reshape(-1)
    weights = packed[:, :, 1:].reshape(-1, 4)
    profile = None
    for corner, offset in enumerate((0, 1, lon_dev, lon_dev + 1)):
        picked = table.at[where + offset].get(mode="promise_in_bounds")
        term = weights[:, corner, None] * picked
        profile = term if profile is None else profile + term
    profile = profile.reshape(-1, trials, kpad).astype(jnp.bfloat16)
    operator = jnp.pad(obs_operator, ((0, 0), (0, extra)))
    evolved = jnp.einsum(
        "rtk,ck->rtc", profile, operator, preferred_element_type=f32
    ).reshape(devices_all, capacity, trials, channels)
    returned = lax.all_to_all(evolved, ("band", "sector"), 0, 0, tiled=True)

    observed = obs_values.reshape(devices_all, capacity, 1, channels)
    inverse = obs_inv_err.reshape(devices_all, capacity, 1, channels)
    live = counts[0][:, None] > jnp.arange(capacity, dtype=jnp.int32)[None, :]
    weighted = (returned - observed) * inverse
    departures = jnp.where(live[:, :, None, None], weighted, 0.0)
    misfit = jnp.sum(departures * departures, axis=(0, 1, 3))

    totals = xor_total(jnp.stack([background, misfit]), ("sector", "band"))
    cell_count = num_lines * lat_dev * lon_dev * devices_all
    cost_values = 0.5 * (totals[0] + totals[1]) / cell_count
    return (departures.reshape(devices_all * capacity, trials, channels), cost_values)


def solution(mesh):
    placed = (
        P(None, "band", "sector"),
        P(None, "band", "sector"),
        P(),
        P(),
        P(),
        P(),
        P(),
        P(("band", "sector"), None),
        P(("band", "sector"), None),
        P(("band", "sector")),
        P(("band", "sector"), None),
        P(("band", "sector"), None),
    )
    return jax.shard_map(
        body,
        mesh=mesh,
        in_specs=placed,
        out_specs=(P(("band", "sector"), None, None), P()),
        check_vma=False,
    )
```

```python
import functools

import jax
import jax.numpy as jnp
from jax import lax
from jax.experimental import pallas as pl
from jax.experimental.pallas import tpu as pltpu
from jax.sharding import PartitionSpec as P

LANES = 128
LINE_TILE = 256


def padded_lines(n):
    return -(-n // LINE_TILE) * LINE_TILE


def local_filter_kernel(lat_dev, lon_dev, x_ref, mix_ref, a_ref, b_ref, out_ref, end_ref):
    chunks, rows, _ = out_ref.shape
    block = 256

    def mix_rows(c, carry):
        at = pl.ds(pl.multiple_of(c * block, block), block)
        res = jnp.dot(x_ref[at, :], mix_ref[...], preferred_element_type=jnp.float32)
        for lc in range(chunks):
            out_ref[lc, at, :] = res[:, lc * LANES:(lc + 1) * LANES]
        return carry

    lax.fori_loop(0, rows // block, mix_rows, 0)

    def lon_step(j, states):
        at = pl.ds(j, lat_dev, stride=lon_dev)
        new = []
        for lc in range(chunks):
            state = a_ref[lc] * states[lc] + out_ref[lc, at, :]
            out_ref[lc, at, :] = state
            new.append(state)
        return tuple(new)

    zero = jnp.zeros((lat_dev, LANES), jnp.float32)
    ends = lax.fori_loop(0, lon_dev, lon_step, (zero,) * chunks)
    for lc in range(chunks):
        end_ref[lc] = ends[lc]

    for lc in range(chunks):
        def lat_step(i, state, lc=lc):
            at = pl.ds(pl.multiple_of(i * lon_dev, lon_dev), lon_dev)
            state = b_ref[lc] * state + out_ref[lc, at, :]
            out_ref[lc, at, :] = state
            return state

        lax.fori_loop(1, lat_dev, lat_step, out_ref[lc, pl.ds(0, lon_dev), :])


def local_filter(xt, mix, a_rows, b_rows, lat_dev, lon_dev):
    trials, positions, klen = xt.shape
    kpad = mix.shape[1]
    chunks = kpad // LANES
    flops = 2 * positions * klen * kpad * trials + 4 * trials * positions * kpad
    bytes_accessed = xt.size * 2 + trials * positions * kpad * 4 + mix.size * 2
    return pl.pallas_call(
        functools.partial(local_filter_kernel, lat_dev, lon_dev),
        grid=(trials,),
        in_specs=[
            pl.BlockSpec((None, positions, klen), lambda t: (t, 0, 0)),
            pl.BlockSpec((klen, kpad), lambda t: (0, 0)),
            pl.BlockSpec((chunks, lat_dev, LANES), lambda t: (0, 0, 0)),
            pl.BlockSpec((chunks, lon_dev, LANES), lambda t: (0, 0, 0)),
        ],
        out_specs=[
            pl.BlockSpec((None, chunks, positions, LANES), lambda t: (t, 0, 0, 0)),
            pl.BlockSpec((None, chunks, lat_dev, LANES), lambda t: (t, 0, 0, 0)),
        ],
        out_shape=[
            jax.ShapeDtypeStruct((trials, chunks, positions, LANES), jnp.float32),
            jax.ShapeDtypeStruct((trials, chunks, lat_dev, LANES), jnp.float32),
        ],
        compiler_params=pltpu.CompilerParams(
            dimension_semantics=("arbitrary",), vmem_limit_bytes=48 * 1024 * 1024
        ),
        cost_estimate=pl.CostEstimate(
            flops=flops, bytes_accessed=bytes_accessed, transcendentals=0
        ),
    )(xt, mix, a_rows, b_rows)


def shifted(x, axis, shift):
    n = lax.axis_size(axis)
    return lax.ppermute(x, axis, [(s, (s + shift) % n) for s in range(n)])


def xor_total(x, axes):
    for axis in axes:
        n = lax.axis_size(axis)
        bit = 1
        while bit < n:
            x = x + lax.ppermute(x, axis, [(s, s ^ bit) for s in range(n)])
            bit *= 2
    return x


def body(
    control,
    direction,
    step_lengths,
    level_root,
    lon_decay,
    lat_decay,
    obs_operator,
    obs_values,
    obs_inv_err,
    obs_cols,
    obs_weights,
    counts,
):
    num_lines, lat_dev, lon_dev = control.shape
    trials = step_lengths.shape[0]
    channels = obs_values.shape[1]
    bands = lax.axis_size("band")
    sectors = lax.axis_size("sector")
    devices_all = bands * sectors
    capacity = obs_cols.shape[0] // devices_all
    kpad = padded_lines(num_lines)
    extra = kpad - num_lines
    f32 = jnp.float32

    packed = jnp.concatenate(
        [obs_cols.astype(f32)[:, None], obs_weights], axis=1
    ).reshape(devices_all, capacity, 5)
    packed = lax.all_to_all(packed, ("band", "sector"), 0, 0, tiled=True)

    trial_fields = control[None] + step_lengths[:, None, None, None] * direction[None]
    background = jnp.sum(trial_fields * trial_fields, axis=(1, 2, 3))
    xt = trial_fields.astype(jnp.bfloat16).reshape(trials, num_lines, lat_dev * lon_dev)
    xt = jnp.pad(jnp.transpose(xt, (0, 2, 1)), ((0, 0), (0, 0), (0, extra)))
    mix_t = jnp.pad(level_root, ((0, extra), (0, extra))).T

    a = jnp.pad(lon_decay, (0, extra), constant_values=0.5)
    b = jnp.pad(lat_decay, (0, extra), constant_values=0.5)
    chunks = kpad // LANES

    def by_chunk(v):
        v = v.reshape(v.shape[:-1] + (chunks, LANES))
        return jnp.moveaxis(v, -2, 0)

    a_c = by_chunk(a)
    b_c = by_chunk(b)
    log_a_c = jnp.log(a_c)
    log_b_c = jnp.log(b_c)
    a_rows = jnp.broadcast_to(a_c[:, None, :], (chunks, lat_dev, LANES))
    b_rows = jnp.broadcast_to(b_c[:, None, :], (chunks, lon_dev, LANES))

    local, lon_ends = local_filter(xt, mix_t, a_rows, b_rows, lat_dev, lon_dev)
    local = local.reshape(trials, chunks, lat_dev, lon_dev, LANES)

    per_line = lambda v: v[None, :, None, :]
    carried = shifted(lon_ends, "sector", 1)
    carried = carried + per_line(jnp.exp(log_a_c * lon_dev)) * shifted(lon_ends, "sector", 2)
    span = 2
    while span < sectors:
        gain = jnp.exp(log_a_c * (lon_dev * span))
        carried = carried + per_line(gain) * shifted(carried, "sector", span)
        span *= 2
    loop_gain = 1.0 - jnp.exp(log_a_c * (lon_dev * sectors))
    incoming = carried / per_line(loop_gain)

    rows = []
    state = jnp.zeros((trials, chunks, LANES), f32)
    for i in range(lat_dev):
        state = b_c[None] * state + incoming[:, :, i, :]
        rows.append(state)
    incoming_lat = jnp.stack(rows, axis=2)
    lon_rise = jnp.exp(log_a_c[:, None, :] * jnp.arange(1, lon_dev + 1).astype(f32)[None, :, None])
    lat_rise = jnp.exp(log_b_c[:, None, :] * jnp.arange(1, lat_dev + 1).astype(f32)[None, :, None])
    scale_a = jnp.sqrt(1.0 - a_c * a_c)[:, None, :]
    scale_b = jnp.sqrt(1.0 - b_c * b_c)[:, None, None, :]

    band_end = scale_a * (
        local[:, :, lat_dev - 1] + lon_rise[None] * incoming_lat[:, :, lat_dev - 1, None, :]
    )
    band_ends = lax.all_gather(band_end, "band")
    me = lax.axis_index("band")
    source = jnp.arange(bands)
    power = (me - 1 - source).astype(f32)
    band_weight = jnp.where(
        (source < me)[:, None, None],
        jnp.exp(log_b_c[None] * (lat_dev * power)[:, None, None]),
        0.0,
    )
    entering = jnp.sum(band_weight[:, None, :, None, :] * band_ends, axis=0)

    increment = scale_b * (
        scale_a[:, None] * (local + lon_rise[None, :, None] * incoming_lat[:, :, :, None, :])
        + lat_rise[None, :, :, None, :] * entering[:, :, None, :, :]
    )
    increment = increment.reshape(trials, chunks, lat_dev * lon_dev, LANES)

    where = packed[:, :, 0].astype(jnp.int32).reshape(-1, 1)
    weights = packed[:, :, 1:].reshape(-1, 4)
    position = jnp.arange(lat_dev * lon_dev, dtype=jnp.int32)[None, :]
    interp = None
    for corner, offset in enumerate((0, 1, lon_dev, lon_dev + 1)):
        term = jnp.where(position == where + offset, weights[:, corner, None], 0.0)
        interp = term if interp is None else interp + term
    profile = jnp.einsum(
        "rp,tcpk->trck", interp, increment, precision=lax.Precision.HIGH,
        preferred_element_type=f32,
    ).astype(jnp.bfloat16)
    operator = jnp.pad(obs_operator, ((0, 0), (0, extra))).reshape(channels, chunks, LANES)
    evolved = jnp.einsum(
        "trck,ock->rto", profile, operator, preferred_element_type=f32
    ).reshape(devices_all, capacity, trials, channels)
    returned = lax.all_to_all(evolved, ("band", "sector"), 0, 0, tiled=True)

    observed = obs_values.reshape(devices_all, capacity, 1, channels)
    inverse = obs_inv_err.reshape(devices_all, capacity, 1, channels)
    live = counts[0][:, None] > jnp.arange(capacity, dtype=jnp.int32)[None, :]
    weighted = (returned - observed) * inverse
    departures = jnp.where(live[:, :, None, None], weighted, 0.0)
    misfit = jnp.sum(departures * departures, axis=(0, 1, 3))

    totals = xor_total(jnp.stack([background, misfit]), ("sector", "band"))
    cell_count = num_lines * lat_dev * lon_dev * devices_all
    cost_values = 0.5 * (totals[0] + totals[1]) / cell_count
    return (departures.reshape(devices_all * capacity, trials, channels), cost_values)


def solution(mesh):
    placed = (
        P(None, "band", "sector"),
        P(None, "band", "sector"),
        P(),
        P(),
        P(),
        P(),
        P(),
        P(("band", "sector"), None),
        P(("band", "sector"), None),
        P(("band", "sector")),
        P(("band", "sector"), None),
        P(("band", "sector"), None),
    )
    return jax.shard_map(
        body,
        mesh=mesh,
        in_specs=placed,
        out_specs=(P(("band", "sector"), None, None), P()),
        check_vma=False,
    )
```

```python
import functools

import jax
import jax.numpy as jnp
from jax import lax
from jax.experimental import pallas as pl
from jax.experimental.pallas import tpu as pltpu
from jax.sharding import PartitionSpec as P

LANES = 128
LINE_TILE = 256


def padded_lines(n):
    return -(-n // LINE_TILE) * LINE_TILE


def local_filter_kernel(lat_dev, lon_dev, x_ref, mix_ref, a_ref, b_ref, out_ref, end_ref, work):
    chunks, rows, _ = out_ref.shape
    block = 256

    def mix_rows(c, carry):
        at = pl.ds(pl.multiple_of(c * block, block), block)
        res = jnp.dot(x_ref[at, :], mix_ref[...], preferred_element_type=jnp.float32)
        for lc in range(chunks):
            work[lc, at, :] = res[:, lc * LANES:(lc + 1) * LANES]
        return carry

    lax.fori_loop(0, rows // block, mix_rows, 0)

    def lon_step(j, states):
        at = pl.ds(pl.multiple_of(j * lat_dev, lat_dev), lat_dev)
        new = []
        for lc in range(chunks):
            state = a_ref[lc] * states[lc] + work[lc, at, :]
            work[lc, at, :] = state
            new.append(state)
        return tuple(new)

    zero = jnp.zeros((lat_dev, LANES), jnp.float32)
    ends = lax.fori_loop(0, lon_dev, lon_step, (zero,) * chunks)
    for lc in range(chunks):
        end_ref[lc] = ends[lc]

    for lc in range(chunks):
        first = work[lc, pl.ds(0, lon_dev, stride=lat_dev), :]
        out_ref[lc, pl.ds(0, lon_dev), :] = first

        def lat_step(i, state, lc=lc):
            state = b_ref[lc] * state + work[lc, pl.ds(i, lon_dev, stride=lat_dev), :]
            out_ref[lc, pl.ds(pl.multiple_of(i * lon_dev, lon_dev), lon_dev), :] = state
            return state

        lax.fori_loop(1, lat_dev, lat_step, first)


def local_filter(xt, mix, a_rows, b_rows, lat_dev, lon_dev):
    trials, positions, klen = xt.shape
    kpad = mix.shape[1]
    chunks = kpad // LANES
    flops = 2 * positions * klen * kpad * trials + 4 * trials * positions * kpad
    bytes_accessed = xt.size * 2 + trials * positions * kpad * 4 + mix.size * 2
    return pl.pallas_call(
        functools.partial(local_filter_kernel, lat_dev, lon_dev),
        grid=(trials,),
        in_specs=[
            pl.BlockSpec((None, positions, klen), lambda t: (t, 0, 0)),
            pl.BlockSpec((klen, kpad), lambda t: (0, 0)),
            pl.BlockSpec((chunks, lat_dev, LANES), lambda t: (0, 0, 0)),
            pl.BlockSpec((chunks, lon_dev, LANES), lambda t: (0, 0, 0)),
        ],
        out_specs=[
            pl.BlockSpec((None, chunks, positions, LANES), lambda t: (t, 0, 0, 0)),
            pl.BlockSpec((None, chunks, lat_dev, LANES), lambda t: (t, 0, 0, 0)),
        ],
        out_shape=[
            jax.ShapeDtypeStruct((trials, chunks, positions, LANES), jnp.float32),
            jax.ShapeDtypeStruct((trials, chunks, lat_dev, LANES), jnp.float32),
        ],
        scratch_shapes=[pltpu.VMEM((chunks, positions, LANES), jnp.float32)],
        compiler_params=pltpu.CompilerParams(
            dimension_semantics=("arbitrary",), vmem_limit_bytes=48 * 1024 * 1024
        ),
        cost_estimate=pl.CostEstimate(
            flops=flops, bytes_accessed=bytes_accessed, transcendentals=0
        ),
    )(xt, mix, a_rows, b_rows)


def shifted(x, axis, shift):
    n = lax.axis_size(axis)
    return lax.ppermute(x, axis, [(s, (s + shift) % n) for s in range(n)])


def xor_total(x, axes):
    for axis in axes:
        n = lax.axis_size(axis)
        bit = 1
        while bit < n:
            x = x + lax.ppermute(x, axis, [(s, s ^ bit) for s in range(n)])
            bit *= 2
    return x


def body(
    control,
    direction,
    step_lengths,
    level_root,
    lon_decay,
    lat_decay,
    obs_operator,
    obs_values,
    obs_inv_err,
    obs_cols,
    obs_weights,
    counts,
):
    num_lines, lat_dev, lon_dev = control.shape
    trials = step_lengths.shape[0]
    channels = obs_values.shape[1]
    bands = lax.axis_size("band")
    sectors = lax.axis_size("sector")
    devices_all = bands * sectors
    capacity = obs_cols.shape[0] // devices_all
    kpad = padded_lines(num_lines)
    extra = kpad - num_lines
    f32 = jnp.float32

    packed = jnp.concatenate(
        [obs_cols.astype(f32)[:, None], obs_weights], axis=1
    ).reshape(devices_all, capacity, 5)
    packed = lax.all_gather(packed, ("band", "sector"))
    packed = lax.dynamic_index_in_dim(packed, lax.axis_index(("band", "sector")), 1, False)

    trial_fields = control[None] + step_lengths[:, None, None, None] * direction[None]
    background = jnp.sum(trial_fields * trial_fields, axis=(1, 2, 3))
    xt = jnp.transpose(trial_fields.astype(jnp.bfloat16), (0, 3, 2, 1))
    xt = jnp.pad(xt.reshape(trials, lon_dev * lat_dev, num_lines), ((0, 0), (0, 0), (0, extra)))
    mix_t = jnp.pad(level_root, ((0, extra), (0, extra))).T

    a = jnp.pad(lon_decay, (0, extra), constant_values=0.5)
    b = jnp.pad(lat_decay, (0, extra), constant_values=0.5)
    chunks = kpad // LANES

    def by_chunk(v):
        v = v.reshape(v.shape[:-1] + (chunks, LANES))
        return jnp.moveaxis(v, -2, 0)

    a_c = by_chunk(a)
    b_c = by_chunk(b)
    log_a_c = jnp.log(a_c)
    log_b_c = jnp.log(b_c)
    a_rows = jnp.broadcast_to(a_c[:, None, :], (chunks, lat_dev, LANES))
    b_rows = jnp.broadcast_to(b_c[:, None, :], (chunks, lon_dev, LANES))

    local, lon_ends = local_filter(xt, mix_t, a_rows, b_rows, lat_dev, lon_dev)
    local = local.reshape(trials, chunks, lat_dev, lon_dev, LANES)

    per_line = lambda v: v[None, :, None, :]
    carried = shifted(lon_ends, "sector", 1)
    carried = carried + per_line(jnp.exp(log_a_c * lon_dev)) * shifted(lon_ends, "sector", 2)
    span = 2
    while span < sectors:
        gain = jnp.exp(log_a_c * (lon_dev * span))
        carried = carried + per_line(gain) * shifted(carried, "sector", span)
        span *= 2
    loop_gain = 1.0 - jnp.exp(log_a_c * (lon_dev * sectors))
    incoming = carried / per_line(loop_gain)

    rows = []
    state = jnp.zeros((trials, chunks, LANES), f32)
    for i in range(lat_dev):
        state = b_c[None] * state + incoming[:, :, i, :]
        rows.append(state)
    incoming_lat = jnp.stack(rows, axis=2)
    lon_rise = jnp.exp(log_a_c[:, None, :] * jnp.arange(1, lon_dev + 1).astype(f32)[None, :, None])
    lat_rise = jnp.exp(log_b_c[:, None, :] * jnp.arange(1, lat_dev + 1).astype(f32)[None, :, None])
    scale_a = jnp.sqrt(1.0 - a_c * a_c)[:, None, :]
    scale_b = jnp.sqrt(1.0 - b_c * b_c)[:, None, None, :]

    band_end = scale_a * (
        local[:, :, lat_dev - 1] + lon_rise[None] * incoming_lat[:, :, lat_dev - 1, None, :]
    )
    band_ends = lax.all_gather(band_end, "band")
    me = lax.axis_index("band")
    source = jnp.arange(bands)
    power = (me - 1 - source).astype(f32)
    band_weight = jnp.where(
        (source < me)[:, None, None],
        jnp.exp(log_b_c[None] * (lat_dev * power)[:, None, None]),
        0.0,
    )
    entering = jnp.sum(band_weight[:, None, :, None, :] * band_ends, axis=0)

    increment = scale_b * (
        scale_a[:, None] * (local + lon_rise[None, :, None] * incoming_lat[:, :, :, None, :])
        + lat_rise[None, :, :, None, :] * entering[:, :, None, :, :]
    )
    increment = increment.reshape(trials, chunks, lat_dev * lon_dev, LANES)

    where = packed[:, :, 0].astype(jnp.int32).reshape(-1, 1)
    weights = packed[:, :, 1:].reshape(-1, 4)
    position = jnp.arange(lat_dev * lon_dev, dtype=jnp.int32)[None, :]
    interp = None
    for corner, offset in enumerate((0, 1, lon_dev, lon_dev + 1)):
        term = jnp.where(position == where + offset, weights[:, corner, None], 0.0)
        interp = term if interp is None else interp + term
    profile = jnp.einsum(
        "tcpk,rp->tckr", increment, interp, precision=lax.Precision.HIGH,
        preferred_element_type=f32,
    ).astype(jnp.bfloat16)
    operator = jnp.pad(obs_operator, ((0, 0), (0, extra))).reshape(channels, chunks, LANES)
    evolved = jnp.einsum(
        "ock,tckr->tor", operator, profile, preferred_element_type=f32
    )
    evolved = jnp.transpose(evolved, (2, 0, 1)).reshape(devices_all, capacity, trials, channels)
    returned = lax.all_to_all(evolved, ("band", "sector"), 0, 0, tiled=True)

    observed = obs_values.reshape(devices_all, capacity, 1, channels)
    inverse = obs_inv_err.reshape(devices_all, capacity, 1, channels)
    live = counts[0][:, None] > jnp.arange(capacity, dtype=jnp.int32)[None, :]
    weighted = (returned - observed) * inverse
    departures = jnp.where(live[:, :, None, None], weighted, 0.0)
    misfit = jnp.sum(departures * departures, axis=(0, 1, 3))

    totals = xor_total(jnp.stack([background, misfit]), ("sector", "band"))
    cell_count = num_lines * lat_dev * lon_dev * devices_all
    cost_values = 0.5 * (totals[0] + totals[1]) / cell_count
    return (departures.reshape(devices_all * capacity, trials, channels), cost_values)


def solution(mesh):
    placed = (
        P(None, "band", "sector"),
        P(None, "band", "sector"),
        P(),
        P(),
        P(),
        P(),
        P(),
        P(("band", "sector"), None),
        P(("band", "sector"), None),
        P(("band", "sector")),
        P(("band", "sector"), None),
        P(("band", "sector"), None),
    )
    return jax.shard_map(
        body,
        mesh=mesh,
        in_specs=placed,
        out_specs=(P(("band", "sector"), None, None), P()),
        check_vma=False,
    )
```

```python
import functools

import jax
import jax.numpy as jnp
from jax import lax
from jax.experimental import pallas as pl
from jax.experimental.pallas import tpu as pltpu
from jax.sharding import PartitionSpec as P

LANES = 128
LINE_TILE = 256


def padded_lines(n):
    return -(-n // LINE_TILE) * LINE_TILE


def local_filter_kernel(lat_dev, lon_dev, steps_ref, c_ref, d_ref, mix_ref, a_ref, b_ref,
                        out_ref, end_ref, grid_rows, lon_rows):
    chunks = out_ref.shape[0]
    lines = mix_ref.shape[0]
    step = steps_ref[pl.program_id(0)]

    def mix_lat(i, carry):
        at = pl.ds(i, lines, stride=lat_dev)
        field = (c_ref[at, :] + step * d_ref[at, :]).astype(jnp.bfloat16)
        res = lax.dot_general(
            field, mix_ref[...], (((0,), (0,)), ((), ())), preferred_element_type=jnp.float32
        )
        rows = pl.ds(pl.multiple_of(i * lon_dev, lon_dev), lon_dev)
        for lc in range(chunks):
            grid_rows[lc, rows, :] = res[:, lc * LANES:(lc + 1) * LANES]
        return carry

    lax.fori_loop(0, lat_dev, mix_lat, 0)

    def lon_step(j, states):
        src = pl.ds(j, lat_dev, stride=lon_dev)
        dst = pl.ds(pl.multiple_of(j * lat_dev, lat_dev), lat_dev)
        new = []
        for lc in range(chunks):
            state = a_ref[lc] * states[lc] + grid_rows[lc, src, :]
            lon_rows[lc, dst, :] = state
            new.append(state)
        return tuple(new)

    zero = jnp.zeros((lat_dev, LANES), jnp.float32)
    ends = lax.fori_loop(0, lon_dev, lon_step, (zero,) * chunks)
    for lc in range(chunks):
        end_ref[lc] = ends[lc]

    for lc in range(chunks):
        first = lon_rows[lc, pl.ds(0, lon_dev, stride=lat_dev), :]
        out_ref[lc, pl.ds(0, lon_dev), :] = first

        def lat_step(i, state, lc=lc):
            state = b_ref[lc] * state + lon_rows[lc, pl.ds(i, lon_dev, stride=lat_dev), :]
            out_ref[lc, pl.ds(pl.multiple_of(i * lon_dev, lon_dev), lon_dev), :] = state
            return state

        lax.fori_loop(1, lat_dev, lat_step, first)


def local_filter(steps, c2, d2, mix, a_rows, b_rows, lat_dev, lon_dev):
    trials = steps.shape[0]
    lines, kpad = mix.shape
    positions = lat_dev * lon_dev
    chunks = kpad // LANES
    flops = 2 * positions * lines * kpad * trials + 4 * trials * positions * kpad
    bytes_accessed = (c2.size + d2.size) * 4 + trials * positions * kpad * 4 + mix.size * 2
    whole = lambda t: (0, 0)
    once = pl.Buffered(1)
    return pl.pallas_call(
        functools.partial(local_filter_kernel, lat_dev, lon_dev),
        grid=(trials,),
        in_specs=[
            pl.BlockSpec(memory_space=pltpu.SMEM),
            pl.BlockSpec(c2.shape, whole, pipeline_mode=once),
            pl.BlockSpec(d2.shape, whole, pipeline_mode=once),
            pl.BlockSpec(mix.shape, whole, pipeline_mode=once),
            pl.BlockSpec((chunks, lat_dev, LANES), lambda t: (0, 0, 0), pipeline_mode=once),
            pl.BlockSpec((chunks, lon_dev, LANES), lambda t: (0, 0, 0), pipeline_mode=once),
        ],
        out_specs=[
            pl.BlockSpec((None, chunks, positions, LANES), lambda t: (t, 0, 0, 0)),
            pl.BlockSpec((None, chunks, lat_dev, LANES), lambda t: (t, 0, 0, 0)),
        ],
        out_shape=[
            jax.ShapeDtypeStruct((trials, chunks, positions, LANES), jnp.float32),
            jax.ShapeDtypeStruct((trials, chunks, lat_dev, LANES), jnp.float32),
        ],
        scratch_shapes=[
            pltpu.VMEM((chunks, positions, LANES), jnp.float32),
            pltpu.VMEM((chunks, positions, LANES), jnp.float32),
        ],
        compiler_params=pltpu.CompilerParams(
            dimension_semantics=("arbitrary",), vmem_limit_bytes=60 * 1024 * 1024
        ),
        cost_estimate=pl.CostEstimate(
            flops=flops, bytes_accessed=bytes_accessed, transcendentals=0
        ),
    )(steps, c2, d2, mix, a_rows, b_rows)


def shifted(x, axis, shift):
    n = lax.axis_size(axis)
    return lax.ppermute(x, axis, [(s, (s + shift) % n) for s in range(n)])


def xor_total(x, axes):
    for axis in axes:
        n = lax.axis_size(axis)
        bit = 1
        while bit < n:
            x = x + lax.ppermute(x, axis, [(s, s ^ bit) for s in range(n)])
            bit *= 2
    return x


def body(
    control,
    direction,
    step_lengths,
    level_root,
    lon_decay,
    lat_decay,
    obs_operator,
    obs_values,
    obs_inv_err,
    obs_cols,
    obs_weights,
    counts,
):
    num_lines, lat_dev, lon_dev = control.shape
    trials = step_lengths.shape[0]
    channels = obs_values.shape[1]
    bands = lax.axis_size("band")
    sectors = lax.axis_size("sector")
    devices_all = bands * sectors
    capacity = obs_cols.shape[0] // devices_all
    kpad = padded_lines(num_lines)
    extra = kpad - num_lines
    f32 = jnp.float32

    packed = jnp.concatenate(
        [obs_cols.astype(f32)[:, None], obs_weights], axis=1
    ).reshape(devices_all, capacity, 5)
    packed = lax.all_gather(packed, ("band", "sector"))
    packed = lax.dynamic_index_in_dim(packed, lax.axis_index(("band", "sector")), 1, False)

    trial_fields = control[None] + step_lengths[:, None, None, None] * direction[None]
    background = jnp.sum(trial_fields * trial_fields, axis=(1, 2, 3))
    mix_t = jnp.pad(level_root.T, ((0, 0), (0, extra)))

    a = jnp.pad(lon_decay, (0, extra), constant_values=0.5)
    b = jnp.pad(lat_decay, (0, extra), constant_values=0.5)
    chunks = kpad // LANES

    def by_chunk(v):
        v = v.reshape(v.shape[:-1] + (chunks, LANES))
        return jnp.moveaxis(v, -2, 0)

    a_c = by_chunk(a)
    b_c = by_chunk(b)
    log_a_c = jnp.log(a_c)
    log_b_c = jnp.log(b_c)
    a_rows = jnp.broadcast_to(a_c[:, None, :], (chunks, lat_dev, LANES))
    b_rows = jnp.broadcast_to(b_c[:, None, :], (chunks, lon_dev, LANES))

    c2 = control.reshape(num_lines * lat_dev, lon_dev)
    d2 = direction.reshape(num_lines * lat_dev, lon_dev)
    local, lon_ends = local_filter(step_lengths, c2, d2, mix_t, a_rows, b_rows, lat_dev, lon_dev)
    local = local.reshape(trials, chunks, lat_dev, lon_dev, LANES)

    per_line = lambda v: v[None, :, None, :]
    carried = shifted(lon_ends, "sector", 1)
    carried = carried + per_line(jnp.exp(log_a_c * lon_dev)) * shifted(lon_ends, "sector", 2)
    span = 2
    while span < sectors:
        gain = jnp.exp(log_a_c * (lon_dev * span))
        carried = carried + per_line(gain) * shifted(carried, "sector", span)
        span *= 2
    loop_gain = 1.0 - jnp.exp(log_a_c * (lon_dev * sectors))
    incoming = carried / per_line(loop_gain)

    rows = []
    state = jnp.zeros((trials, chunks, LANES), f32)
    for i in range(lat_dev):
        state = b_c[None] * state + incoming[:, :, i, :]
        rows.append(state)
    incoming_lat = jnp.stack(rows, axis=2)
    lon_rise = jnp.exp(log_a_c[:, None, :] * jnp.arange(1, lon_dev + 1).astype(f32)[None, :, None])
    lat_rise = jnp.exp(log_b_c[:, None, :] * jnp.arange(1, lat_dev + 1).astype(f32)[None, :, None])
    scale_a = jnp.sqrt(1.0 - a_c * a_c)[:, None, :]
    scale_b = jnp.sqrt(1.0 - b_c * b_c)[:, None, None, :]

    band_end = scale_a * (
        local[:, :, lat_dev - 1] + lon_rise[None] * incoming_lat[:, :, lat_dev - 1, None, :]
    )
    band_ends = lax.all_gather(band_end, "band")
    me = lax.axis_index("band")
    source = jnp.arange(bands)
    power = (me - 1 - source).astype(f32)
    band_weight = jnp.where(
        (source < me)[:, None, None],
        jnp.exp(log_b_c[None] * (lat_dev * power)[:, None, None]),
        0.0,
    )
    entering = jnp.sum(band_weight[:, None, :, None, :] * band_ends, axis=0)

    increment = scale_b * (
        scale_a[:, None] * (local + lon_rise[None, :, None] * incoming_lat[:, :, :, None, :])
        + lat_rise[None, :, :, None, :] * entering[:, :, None, :, :]
    )
    increment = increment.reshape(trials, chunks, lat_dev * lon_dev, LANES)

    where = packed[:, :, 0].astype(jnp.int32).reshape(-1, 1)
    weights = packed[:, :, 1:].reshape(-1, 4)
    position = jnp.arange(lat_dev * lon_dev, dtype=jnp.int32)[None, :]
    interp = None
    for corner, offset in enumerate((0, 1, lon_dev, lon_dev + 1)):
        term = jnp.where(position == where + offset, weights[:, corner, None], 0.0)
        interp = term if interp is None else interp + term
    profile = jnp.einsum(
        "tcpk,rp->tckr", increment, interp, precision=lax.Precision.HIGH,
        preferred_element_type=f32,
    ).astype(jnp.bfloat16)
    operator = jnp.pad(obs_operator, ((0, 0), (0, extra))).reshape(channels, chunks, LANES)
    evolved = jnp.einsum(
        "ock,tckr->tor", operator, profile, preferred_element_type=f32
    )
    evolved = jnp.transpose(evolved, (2, 0, 1)).reshape(devices_all, capacity, trials, channels)
    returned = lax.all_to_all(evolved, ("band", "sector"), 0, 0, tiled=True)

    observed = obs_values.reshape(devices_all, capacity, 1, channels)
    inverse = obs_inv_err.reshape(devices_all, capacity, 1, channels)
    live = counts[0][:, None] > jnp.arange(capacity, dtype=jnp.int32)[None, :]
    weighted = (returned - observed) * inverse
    departures = jnp.where(live[:, :, None, None], weighted, 0.0)
    misfit = jnp.sum(departures * departures, axis=(0, 1, 3))

    totals = xor_total(jnp.stack([background, misfit]), ("sector", "band"))
    cell_count = num_lines * lat_dev * lon_dev * devices_all
    cost_values = 0.5 * (totals[0] + totals[1]) / cell_count
    return (departures.reshape(devices_all * capacity, trials, channels), cost_values)


def solution(mesh):
    placed = (
        P(None, "band", "sector"),
        P(None, "band", "sector"),
        P(),
        P(),
        P(),
        P(),
        P(),
        P(("band", "sector"), None),
        P(("band", "sector"), None),
        P(("band", "sector")),
        P(("band", "sector"), None),
        P(("band", "sector"), None),
    )
    return jax.shard_map(
        body,
        mesh=mesh,
        in_specs=placed,
        out_specs=(P(("band", "sector"), None, None), P()),
        check_vma=False,
    )
```

```python
import functools

import jax
import jax.numpy as jnp
from jax import lax
from jax.experimental import pallas as pl
from jax.experimental.pallas import tpu as pltpu
from jax.sharding import PartitionSpec as P

LANES = 128
LINE_TILE = 256


def padded_lines(n):
    return -(-n // LINE_TILE) * LINE_TILE


def local_filter_kernel(lat_dev, lon_dev, x_ref, mix_ref, a_ref, b_ref, out_ref, end_ref, work):
    chunks, rows, _ = out_ref.shape
    block = 256

    def mix_rows(c, carry):
        at = pl.ds(pl.multiple_of(c * block, block), block)
        res = jnp.dot(x_ref[at, :], mix_ref[...], preferred_element_type=jnp.float32)
        for lc in range(chunks):
            work[lc, at, :] = res[:, lc * LANES:(lc + 1) * LANES]
        return carry

    lax.fori_loop(0, rows // block, mix_rows, 0)

    def lon_step(j, states):
        at = pl.ds(pl.multiple_of(j * lat_dev, lat_dev), lat_dev)
        new = []
        for lc in range(chunks):
            state = a_ref[lc] * states[lc] + work[lc, at, :]
            work[lc, at, :] = state
            new.append(state)
        return tuple(new)

    zero = jnp.zeros((lat_dev, LANES), jnp.float32)
    ends = lax.fori_loop(0, lon_dev, lon_step, (zero,) * chunks)
    for lc in range(chunks):
        end_ref[lc] = ends[lc]

    for lc in range(chunks):
        first = work[lc, pl.ds(0, lon_dev, stride=lat_dev), :]
        out_ref[lc, pl.ds(0, lon_dev), :] = first

        def lat_step(i, state, lc=lc):
            state = b_ref[lc] * state + work[lc, pl.ds(i, lon_dev, stride=lat_dev), :]
            out_ref[lc, pl.ds(pl.multiple_of(i * lon_dev, lon_dev), lon_dev), :] = state
            return state

        lax.fori_loop(1, lat_dev, lat_step, first)


def local_filter(xt, mix, a_rows, b_rows, lat_dev, lon_dev):
    trials, positions, klen = xt.shape
    kpad = mix.shape[1]
    chunks = kpad // LANES
    flops = 2 * positions * klen * kpad * trials + 4 * trials * positions * kpad
    bytes_accessed = xt.size * 2 + trials * positions * kpad * 4 + mix.size * 2
    return pl.pallas_call(
        functools.partial(local_filter_kernel, lat_dev, lon_dev),
        grid=(trials,),
        in_specs=[
            pl.BlockSpec((None, positions, klen), lambda t: (t, 0, 0)),
            pl.BlockSpec((klen, kpad), lambda t: (0, 0)),
            pl.BlockSpec((chunks, lat_dev, LANES), lambda t: (0, 0, 0)),
            pl.BlockSpec((chunks, lon_dev, LANES), lambda t: (0, 0, 0)),
        ],
        out_specs=[
            pl.BlockSpec((None, chunks, positions, LANES), lambda t: (t, 0, 0, 0)),
            pl.BlockSpec((None, chunks, lat_dev, LANES), lambda t: (t, 0, 0, 0)),
        ],
        out_shape=[
            jax.ShapeDtypeStruct((trials, chunks, positions, LANES), jnp.float32),
            jax.ShapeDtypeStruct((trials, chunks, lat_dev, LANES), jnp.float32),
        ],
        scratch_shapes=[pltpu.VMEM((chunks, positions, LANES), jnp.float32)],
        compiler_params=pltpu.CompilerParams(
            dimension_semantics=("arbitrary",), vmem_limit_bytes=48 * 1024 * 1024
        ),
        cost_estimate=pl.CostEstimate(
            flops=flops, bytes_accessed=bytes_accessed, transcendentals=0
        ),
    )(xt, mix, a_rows, b_rows)


def shifted(x, axis, shift):
    n = lax.axis_size(axis)
    return lax.ppermute(x, axis, [(s, (s + shift) % n) for s in range(n)])


def xor_total(x, axes):
    for axis in axes:
        n = lax.axis_size(axis)
        bit = 1
        while bit < n:
            x = x + lax.ppermute(x, axis, [(s, s ^ bit) for s in range(n)])
            bit *= 2
    return x


def body(
    control,
    direction,
    step_lengths,
    level_root,
    lon_decay,
    lat_decay,
    obs_operator,
    obs_values,
    obs_inv_err,
    obs_cols,
    obs_weights,
    counts,
):
    num_lines, lat_dev, lon_dev = control.shape
    trials = step_lengths.shape[0]
    channels = obs_values.shape[1]
    bands = lax.axis_size("band")
    sectors = lax.axis_size("sector")
    devices_all = bands * sectors
    capacity = obs_cols.shape[0] // devices_all
    kpad = padded_lines(num_lines)
    extra = kpad - num_lines
    f32 = jnp.float32

    packed = jnp.concatenate(
        [obs_cols.astype(f32)[:, None], obs_weights], axis=1
    ).reshape(devices_all, capacity, 5)
    packed = lax.all_gather(packed, ("band", "sector"))
    packed = lax.dynamic_index_in_dim(packed, lax.axis_index(("band", "sector")), 1, False)

    trial_fields = control[None] + step_lengths[:, None, None, None] * direction[None]
    background = jnp.sum(trial_fields * trial_fields, axis=(1, 2, 3))
    xt = jnp.transpose(trial_fields.astype(jnp.bfloat16), (0, 3, 2, 1))
    xt = jnp.pad(xt.reshape(trials, lon_dev * lat_dev, num_lines), ((0, 0), (0, 0), (0, extra)))
    mix_t = jnp.pad(level_root, ((0, extra), (0, extra))).T

    a = jnp.pad(lon_decay, (0, extra), constant_values=0.5)
    b = jnp.pad(lat_decay, (0, extra), constant_values=0.5)
    chunks = kpad // LANES

    def by_chunk(v):
        v = v.reshape(v.shape[:-1] + (chunks, LANES))
        return jnp.moveaxis(v, -2, 0)

    a_c = by_chunk(a)
    b_c = by_chunk(b)
    log_a_c = jnp.log(a_c)
    log_b_c = jnp.log(b_c)
    a_rows = jnp.broadcast_to(a_c[:, None, :], (chunks, lat_dev, LANES))
    b_rows = jnp.broadcast_to(b_c[:, None, :], (chunks, lon_dev, LANES))

    local, lon_ends = local_filter(xt, mix_t, a_rows, b_rows, lat_dev, lon_dev)
    local = local.reshape(trials, chunks, lat_dev, lon_dev, LANES)

    per_line = lambda v: v[None, :, None, :]
    carried = shifted(lon_ends, "sector", 1)
    carried = carried + per_line(jnp.exp(log_a_c * lon_dev)) * shifted(lon_ends, "sector", 2)
    span = 2
    while span < sectors:
        gain = jnp.exp(log_a_c * (lon_dev * span))
        carried = carried + per_line(gain) * shifted(carried, "sector", span)
        span *= 2
    loop_gain = 1.0 - jnp.exp(log_a_c * (lon_dev * sectors))
    incoming = carried / per_line(loop_gain)

    rows = []
    state = jnp.zeros((trials, chunks, LANES), f32)
    for i in range(lat_dev):
        state = b_c[None] * state + incoming[:, :, i, :]
        rows.append(state)
    incoming_lat = jnp.stack(rows, axis=2)
    lon_rise = jnp.exp(log_a_c[:, None, :] * jnp.arange(1, lon_dev + 1).astype(f32)[None, :, None])
    lat_rise = jnp.exp(log_b_c[:, None, :] * jnp.arange(1, lat_dev + 1).astype(f32)[None, :, None])
    scale_a = jnp.sqrt(1.0 - a_c * a_c)[:, None, :]
    scale_b = jnp.sqrt(1.0 - b_c * b_c)[:, None, None, :]

    band_end = scale_a * (
        local[:, :, lat_dev - 1] + lon_rise[None] * incoming_lat[:, :, lat_dev - 1, None, :]
    )
    entering = None
    for m in range(1, bands):
        came = lax.ppermute(band_end, "band", [(p, p + m) for p in range(bands - m)])
        term = jnp.exp(log_b_c * (lat_dev * (m - 1)))[None, :, None, :] * came
        entering = term if entering is None else entering + term
    if entering is None:
        entering = jnp.zeros_like(band_end)

    increment = scale_b * (
        scale_a[:, None] * (local + lon_rise[None, :, None] * incoming_lat[:, :, :, None, :])
        + lat_rise[None, :, :, None, :] * entering[:, :, None, :, :]
    )
    increment = jnp.moveaxis(increment.reshape(trials, chunks, lat_dev * lon_dev, LANES), 1, 2)
    increment = increment.reshape(trials, lat_dev * lon_dev, kpad)

    where = packed[:, :, 0].astype(jnp.int32).reshape(-1, 1)
    weights = packed[:, :, 1:].reshape(-1, 4)
    position = jnp.arange(lat_dev * lon_dev, dtype=jnp.int32)[None, :]
    interp = None
    for corner, offset in enumerate((0, 1, lon_dev, lon_dev + 1)):
        term = jnp.where(position == where + offset, weights[:, corner, None], 0.0)
        interp = term if interp is None else interp + term
    profile = jnp.einsum(
        "rp,tpn->trn", interp, increment, precision=lax.Precision.HIGH,
        preferred_element_type=f32,
    ).astype(jnp.bfloat16)
    operator = jnp.pad(obs_operator, ((0, 0), (0, extra)))
    evolved = jnp.einsum(
        "trn,on->rto", profile, operator, preferred_element_type=f32
    ).reshape(devices_all, capacity, trials, channels)
    returned = lax.all_to_all(evolved, ("band", "sector"), 0, 0, tiled=True)

    observed = obs_values.reshape(devices_all, capacity, 1, channels)
    inverse = obs_inv_err.reshape(devices_all, capacity, 1, channels)
    live = counts[0][:, None] > jnp.arange(capacity, dtype=jnp.int32)[None, :]
    weighted = (returned - observed) * inverse
    departures = jnp.where(live[:, :, None, None], weighted, 0.0)
    misfit = jnp.sum(departures * departures, axis=(0, 1, 3))

    totals = xor_total(jnp.stack([background, misfit]), ("sector", "band"))
    cell_count = num_lines * lat_dev * lon_dev * devices_all
    cost_values = 0.5 * (totals[0] + totals[1]) / cell_count
    return (departures.reshape(devices_all * capacity, trials, channels), cost_values)


def solution(mesh):
    placed = (
        P(None, "band", "sector"),
        P(None, "band", "sector"),
        P(),
        P(),
        P(),
        P(),
        P(),
        P(("band", "sector"), None),
        P(("band", "sector"), None),
        P(("band", "sector")),
        P(("band", "sector"), None),
        P(("band", "sector"), None),
    )
    return jax.shard_map(
        body,
        mesh=mesh,
        in_specs=placed,
        out_specs=(P(("band", "sector"), None, None), P()),
        check_vma=False,
    )
```

```python
import functools

import jax
import jax.numpy as jnp
from jax import lax
from jax.experimental import pallas as pl
from jax.experimental.pallas import tpu as pltpu
from jax.sharding import PartitionSpec as P

LANES = 128
LINE_TILE = 256


def padded_lines(n):
    return -(-n // LINE_TILE) * LINE_TILE


def local_filter_kernel(lat_dev, lon_dev, x_ref, mix_ref, a_ref, b_ref, out_ref, end_ref, work):
    chunks, rows, _ = out_ref.shape
    block = 256

    def mix_rows(c, carry):
        at = pl.ds(pl.multiple_of(c * block, block), block)
        res = jnp.dot(x_ref[at, :], mix_ref[...], preferred_element_type=jnp.float32)
        for lc in range(chunks):
            work[lc, at, :] = res[:, lc * LANES:(lc + 1) * LANES]
        return carry

    lax.fori_loop(0, rows // block, mix_rows, 0)

    def lon_step(j, states):
        at = pl.ds(pl.multiple_of(j * lat_dev, lat_dev), lat_dev)
        new = []
        for lc in range(chunks):
            state = a_ref[lc] * states[lc] + work[lc, at, :]
            work[lc, at, :] = state
            new.append(state)
        return tuple(new)

    zero = jnp.zeros((lat_dev, LANES), jnp.float32)
    ends = lax.fori_loop(0, lon_dev, lon_step, (zero,) * chunks)
    for lc in range(chunks):
        end_ref[lc] = ends[lc]

    for lc in range(chunks):
        first = work[lc, pl.ds(0, lon_dev, stride=lat_dev), :]
        out_ref[lc, pl.ds(0, lon_dev), :] = first

        def lat_step(i, state, lc=lc):
            state = b_ref[lc] * state + work[lc, pl.ds(i, lon_dev, stride=lat_dev), :]
            out_ref[lc, pl.ds(pl.multiple_of(i * lon_dev, lon_dev), lon_dev), :] = state
            return state

        lax.fori_loop(1, lat_dev, lat_step, first)


def local_filter(xt, mix, a_rows, b_rows, lat_dev, lon_dev):
    trials, positions, klen = xt.shape
    kpad = mix.shape[1]
    chunks = kpad // LANES
    flops = 2 * positions * klen * kpad * trials + 4 * trials * positions * kpad
    bytes_accessed = xt.size * 2 + trials * positions * kpad * 4 + mix.size * 2
    return pl.pallas_call(
        functools.partial(local_filter_kernel, lat_dev, lon_dev),
        grid=(trials,),
        in_specs=[
            pl.BlockSpec((None, positions, klen), lambda t: (t, 0, 0)),
            pl.BlockSpec((klen, kpad), lambda t: (0, 0)),
            pl.BlockSpec((chunks, lat_dev, LANES), lambda t: (0, 0, 0)),
            pl.BlockSpec((chunks, lon_dev, LANES), lambda t: (0, 0, 0)),
        ],
        out_specs=[
            pl.BlockSpec((None, chunks, positions, LANES), lambda t: (t, 0, 0, 0)),
            pl.BlockSpec((None, chunks, lat_dev, LANES), lambda t: (t, 0, 0, 0)),
        ],
        out_shape=[
            jax.ShapeDtypeStruct((trials, chunks, positions, LANES), jnp.float32),
            jax.ShapeDtypeStruct((trials, chunks, lat_dev, LANES), jnp.float32),
        ],
        scratch_shapes=[pltpu.VMEM((chunks, positions, LANES), jnp.float32)],
        compiler_params=pltpu.CompilerParams(
            dimension_semantics=("arbitrary",), vmem_limit_bytes=48 * 1024 * 1024
        ),
        cost_estimate=pl.CostEstimate(
            flops=flops, bytes_accessed=bytes_accessed, transcendentals=0
        ),
    )(xt, mix, a_rows, b_rows)


def shifted(x, axis, shift):
    n = lax.axis_size(axis)
    return lax.ppermute(x, axis, [(s, (s + shift) % n) for s in range(n)])


def xor_total(x, axes):
    for axis in axes:
        n = lax.axis_size(axis)
        bit = 1
        while bit < n:
            x = x + lax.ppermute(x, axis, [(s, s ^ bit) for s in range(n)])
            bit *= 2
    return x


def body(
    control,
    direction,
    step_lengths,
    level_root,
    lon_decay,
    lat_decay,
    obs_operator,
    obs_values,
    obs_inv_err,
    obs_cols,
    obs_weights,
    counts,
):
    num_lines, lat_dev, lon_dev = control.shape
    trials = step_lengths.shape[0]
    channels = obs_values.shape[1]
    bands = lax.axis_size("band")
    sectors = lax.axis_size("sector")
    devices_all = bands * sectors
    capacity = obs_cols.shape[0] // devices_all
    kpad = padded_lines(num_lines)
    extra = kpad - num_lines
    f32 = jnp.float32

    packed = jnp.concatenate(
        [obs_cols.astype(f32)[:, None], obs_weights], axis=1
    ).reshape(devices_all, capacity, 5)
    packed = lax.all_gather(packed, ("band", "sector"))
    packed = lax.dynamic_index_in_dim(packed, lax.axis_index(("band", "sector")), 1, False)

    trial_fields = control[None] + step_lengths[:, None, None, None] * direction[None]
    background = jnp.sum(trial_fields * trial_fields, axis=(1, 2, 3))
    xt = jnp.transpose(trial_fields.astype(jnp.bfloat16), (0, 3, 2, 1))
    xt = jnp.pad(xt.reshape(trials, lon_dev * lat_dev, num_lines), ((0, 0), (0, 0), (0, extra)))
    mix_t = jnp.pad(level_root, ((0, extra), (0, extra))).T

    a = jnp.pad(lon_decay, (0, extra), constant_values=0.5)
    b = jnp.pad(lat_decay, (0, extra), constant_values=0.5)
    chunks = kpad // LANES

    def by_chunk(v):
        v = v.reshape(v.shape[:-1] + (chunks, LANES))
        return jnp.moveaxis(v, -2, 0)

    a_c = by_chunk(a)
    b_c = by_chunk(b)
    log_a_c = jnp.log(a_c)
    log_b_c = jnp.log(b_c)
    a_rows = jnp.broadcast_to(a_c[:, None, :], (chunks, lat_dev, LANES))
    b_rows = jnp.broadcast_to(b_c[:, None, :], (chunks, lon_dev, LANES))

    local, lon_ends = local_filter(xt, mix_t, a_rows, b_rows, lat_dev, lon_dev)
    local = local.reshape(trials, chunks, lat_dev, lon_dev, LANES)

    per_line = lambda v: v[None, :, None, :]
    carried = shifted(lon_ends, "sector", 1)
    carried = carried + per_line(jnp.exp(log_a_c * lon_dev)) * shifted(lon_ends, "sector", 2)
    span = 2
    while span < sectors:
        gain = jnp.exp(log_a_c * (lon_dev * span))
        carried = carried + per_line(gain) * shifted(carried, "sector", span)
        span *= 2
    loop_gain = 1.0 - jnp.exp(log_a_c * (lon_dev * sectors))
    incoming = carried / per_line(loop_gain)

    rows = []
    state = jnp.zeros((trials, chunks, LANES), f32)
    for i in range(lat_dev):
        state = b_c[None] * state + incoming[:, :, i, :]
        rows.append(state)
    incoming_lat = jnp.stack(rows, axis=2)
    lon_rise = jnp.exp(log_a_c[:, None, :] * jnp.arange(1, lon_dev + 1).astype(f32)[None, :, None])
    lat_rise = jnp.exp(log_b_c[:, None, :] * jnp.arange(1, lat_dev + 1).astype(f32)[None, :, None])
    scale_a = jnp.sqrt(1.0 - a_c * a_c)[:, None, :]
    scale_b = jnp.sqrt(1.0 - b_c * b_c)[:, None, None, :]

    band_end = scale_a * (
        local[:, :, lat_dev - 1] + lon_rise[None] * incoming_lat[:, :, lat_dev - 1, None, :]
    )
    band_ends = lax.all_gather(band_end, "band")
    me = lax.axis_index("band")
    source = jnp.arange(bands)
    power = (me - 1 - source).astype(f32)
    band_weight = jnp.where(
        (source < me)[:, None, None],
        jnp.exp(log_b_c[None] * (lat_dev * power)[:, None, None]),
        0.0,
    )
    entering = jnp.sum(band_weight[:, None, :, None, :] * band_ends, axis=0)

    increment = scale_b * (
        scale_a[:, None] * (local + lon_rise[None, :, None] * incoming_lat[:, :, :, None, :])
        + lat_rise[None, :, :, None, :] * entering[:, :, None, :, :]
    )
    increment = jnp.moveaxis(increment.reshape(trials, chunks, lat_dev * lon_dev, LANES), 1, 2)
    increment = increment.reshape(trials, lat_dev * lon_dev, kpad)

    where = packed[:, :, 0].astype(jnp.int32).reshape(-1, 1)
    weights = packed[:, :, 1:].reshape(-1, 4)
    position = jnp.arange(lat_dev * lon_dev, dtype=jnp.int32)[None, :]
    interp = None
    for corner, offset in enumerate((0, 1, lon_dev, lon_dev + 1)):
        term = jnp.where(position == where + offset, weights[:, corner, None], 0.0)
        interp = term if interp is None else interp + term
    profile = jnp.einsum(
        "rp,tpn->trn", interp, increment, precision=lax.Precision.HIGH,
        preferred_element_type=f32,
    ).astype(jnp.bfloat16)
    operator = jnp.pad(obs_operator, ((0, 0), (0, extra)))
    evolved = jnp.einsum(
        "trn,on->rto", profile, operator, preferred_element_type=f32
    ).reshape(devices_all, capacity, trials, channels)
    returned = lax.all_to_all(evolved, ("band", "sector"), 0, 0, tiled=True)

    observed = obs_values.reshape(devices_all, capacity, 1, channels)
    inverse = obs_inv_err.reshape(devices_all, capacity, 1, channels)
    live = counts[0][:, None] > jnp.arange(capacity, dtype=jnp.int32)[None, :]
    weighted = (returned - observed) * inverse
    departures = jnp.where(live[:, :, None, None], weighted, 0.0)
    misfit = jnp.sum(departures * departures, axis=(0, 1, 3))

    totals = xor_total(jnp.stack([background, misfit]), ("sector", "band"))
    cell_count = num_lines * lat_dev * lon_dev * devices_all
    cost_values = 0.5 * (totals[0] + totals[1]) / cell_count
    return (departures.reshape(devices_all * capacity, trials, channels), cost_values)


def solution(mesh):
    placed = (
        P(None, "band", "sector"),
        P(None, "band", "sector"),
        P(),
        P(),
        P(),
        P(),
        P(),
        P(("band", "sector"), None),
        P(("band", "sector"), None),
        P(("band", "sector")),
        P(("band", "sector"), None),
        P(("band", "sector"), None),
    )
    return jax.shard_map(
        body,
        mesh=mesh,
        in_specs=placed,
        out_specs=(P(("band", "sector"), None, None), P()),
        check_vma=False,
    )
```

```python
import functools

import jax
import jax.numpy as jnp
from jax import lax
from jax.experimental import pallas as pl
from jax.experimental.pallas import tpu as pltpu
from jax.sharding import PartitionSpec as P

LANES = 128
LINE_TILE = 256


def padded_lines(n):
    return -(-n // LINE_TILE) * LINE_TILE


def local_filter_kernel(lat_dev, lon_dev, x_ref, mix_ref, a_ref, b_ref, out_ref, end_ref, work):
    chunks, rows, _ = out_ref.shape
    block = 256

    def mix_rows(c, carry):
        at = pl.ds(pl.multiple_of(c * block, block), block)
        res = jnp.dot(x_ref[at, :], mix_ref[...], preferred_element_type=jnp.float32)
        for lc in range(chunks):
            work[lc, at, :] = res[:, lc * LANES:(lc + 1) * LANES]
        return carry

    lax.fori_loop(0, rows // block, mix_rows, 0)

    def lon_step(j, states):
        at = pl.ds(pl.multiple_of(j * lat_dev, lat_dev), lat_dev)
        new = []
        for lc in range(chunks):
            state = a_ref[lc] * states[lc] + work[lc, at, :]
            work[lc, at, :] = state
            new.append(state)
        return tuple(new)

    zero = jnp.zeros((lat_dev, LANES), jnp.float32)
    ends = lax.fori_loop(0, lon_dev, lon_step, (zero,) * chunks)
    for lc in range(chunks):
        end_ref[lc] = ends[lc]

    for lc in range(chunks):
        first = work[lc, pl.ds(0, lon_dev, stride=lat_dev), :]
        out_ref[lc, pl.ds(0, lon_dev), :] = first

        def lat_step(i, state, lc=lc):
            state = b_ref[lc] * state + work[lc, pl.ds(i, lon_dev, stride=lat_dev), :]
            out_ref[lc, pl.ds(pl.multiple_of(i * lon_dev, lon_dev), lon_dev), :] = state
            return state

        lax.fori_loop(1, lat_dev, lat_step, first)


def local_filter(xt, mix, a_rows, b_rows, lat_dev, lon_dev):
    trials, positions, klen = xt.shape
    kpad = mix.shape[1]
    chunks = kpad // LANES
    flops = 2 * positions * klen * kpad * trials + 4 * trials * positions * kpad
    bytes_accessed = xt.size * 2 + trials * positions * kpad * 4 + mix.size * 2
    return pl.pallas_call(
        functools.partial(local_filter_kernel, lat_dev, lon_dev),
        grid=(trials,),
        in_specs=[
            pl.BlockSpec((None, positions, klen), lambda t: (t, 0, 0)),
            pl.BlockSpec((klen, kpad), lambda t: (0, 0)),
            pl.BlockSpec((chunks, lat_dev, LANES), lambda t: (0, 0, 0)),
            pl.BlockSpec((chunks, lon_dev, LANES), lambda t: (0, 0, 0)),
        ],
        out_specs=[
            pl.BlockSpec((None, chunks, positions, LANES), lambda t: (t, 0, 0, 0)),
            pl.BlockSpec((None, chunks, lat_dev, LANES), lambda t: (t, 0, 0, 0)),
        ],
        out_shape=[
            jax.ShapeDtypeStruct((trials, chunks, positions, LANES), jnp.float32),
            jax.ShapeDtypeStruct((trials, chunks, lat_dev, LANES), jnp.float32),
        ],
        scratch_shapes=[pltpu.VMEM((chunks, positions, LANES), jnp.float32)],
        compiler_params=pltpu.CompilerParams(
            dimension_semantics=("arbitrary",), vmem_limit_bytes=48 * 1024 * 1024
        ),
        cost_estimate=pl.CostEstimate(
            flops=flops, bytes_accessed=bytes_accessed, transcendentals=0
        ),
    )(xt, mix, a_rows, b_rows)


def shifted(x, axis, shift):
    n = lax.axis_size(axis)
    return lax.ppermute(x, axis, [(s, (s + shift) % n) for s in range(n)])


def xor_total(x, axes):
    for axis in axes:
        n = lax.axis_size(axis)
        bit = 1
        while bit < n:
            x = x + lax.ppermute(x, axis, [(s, s ^ bit) for s in range(n)])
            bit *= 2
    return x


def body(
    control,
    direction,
    step_lengths,
    level_root,
    lon_decay,
    lat_decay,
    obs_operator,
    obs_values,
    obs_inv_err,
    obs_cols,
    obs_weights,
    counts,
):
    num_lines, lat_dev, lon_dev = control.shape
    trials = step_lengths.shape[0]
    channels = obs_values.shape[1]
    bands = lax.axis_size("band")
    sectors = lax.axis_size("sector")
    devices_all = bands * sectors
    capacity = obs_cols.shape[0] // devices_all
    kpad = padded_lines(num_lines)
    extra = kpad - num_lines
    f32 = jnp.float32

    packed = jnp.concatenate(
        [obs_cols.astype(f32)[:, None], obs_weights], axis=1
    ).reshape(devices_all, capacity, 5)
    packed = lax.all_gather(packed, ("band", "sector"))
    packed = lax.dynamic_index_in_dim(packed, lax.axis_index(("band", "sector")), 1, False)

    trial_fields = control[None] + step_lengths[:, None, None, None] * direction[None]
    background = jnp.sum(trial_fields * trial_fields, axis=(1, 2, 3))
    xt = jnp.transpose(trial_fields.astype(jnp.bfloat16), (0, 3, 2, 1))
    xt = xt.reshape(trials, lon_dev * lat_dev, num_lines)
    mix_t = jnp.pad(level_root, ((0, extra), (0, 0))).T

    a = jnp.pad(lon_decay, (0, extra), constant_values=0.5)
    b = jnp.pad(lat_decay, (0, extra), constant_values=0.5)
    chunks = kpad // LANES

    def by_chunk(v):
        v = v.reshape(v.shape[:-1] + (chunks, LANES))
        return jnp.moveaxis(v, -2, 0)

    a_c = by_chunk(a)
    b_c = by_chunk(b)
    log_a_c = jnp.log(a_c)
    log_b_c = jnp.log(b_c)
    a_rows = jnp.broadcast_to(a_c[:, None, :], (chunks, lat_dev, LANES))
    b_rows = jnp.broadcast_to(b_c[:, None, :], (chunks, lon_dev, LANES))

    local, lon_ends = local_filter(xt, mix_t, a_rows, b_rows, lat_dev, lon_dev)
    local = local.reshape(trials, chunks, lat_dev, lon_dev, LANES)

    per_line = lambda v: v[None, :, None, :]
    carried = shifted(lon_ends, "sector", 1)
    carried = carried + per_line(jnp.exp(log_a_c * lon_dev)) * shifted(lon_ends, "sector", 2)
    span = 2
    while span < sectors:
        gain = jnp.exp(log_a_c * (lon_dev * span))
        carried = carried + per_line(gain) * shifted(carried, "sector", span)
        span *= 2
    loop_gain = 1.0 - jnp.exp(log_a_c * (lon_dev * sectors))
    incoming = carried / per_line(loop_gain)

    rows = []
    state = jnp.zeros((trials, chunks, LANES), f32)
    for i in range(lat_dev):
        state = b_c[None] * state + incoming[:, :, i, :]
        rows.append(state)
    incoming_lat = jnp.stack(rows, axis=2)
    lon_rise = jnp.exp(log_a_c[:, None, :] * jnp.arange(1, lon_dev + 1).astype(f32)[None, :, None])
    lat_rise = jnp.exp(log_b_c[:, None, :] * jnp.arange(1, lat_dev + 1).astype(f32)[None, :, None])
    scale_a = jnp.sqrt(1.0 - a_c * a_c)[:, None, :]
    scale_b = jnp.sqrt(1.0 - b_c * b_c)[:, None, None, :]

    band_end = scale_a * (
        local[:, :, lat_dev - 1] + lon_rise[None] * incoming_lat[:, :, lat_dev - 1, None, :]
    )
    band_ends = lax.all_gather(band_end, "band")
    me = lax.axis_index("band")
    source = jnp.arange(bands)
    power = (me - 1 - source).astype(f32)
    band_weight = jnp.where(
        (source < me)[:, None, None],
        jnp.exp(log_b_c[None] * (lat_dev * power)[:, None, None]),
        0.0,
    )
    entering = jnp.sum(band_weight[:, None, :, None, :] * band_ends, axis=0)

    increment = scale_b * (
        scale_a[:, None] * (local + lon_rise[None, :, None] * incoming_lat[:, :, :, None, :])
        + lat_rise[None, :, :, None, :] * entering[:, :, None, :, :]
    )
    increment = jnp.moveaxis(increment.reshape(trials, chunks, lat_dev * lon_dev, LANES), 1, 2)
    increment = increment.reshape(trials, lat_dev * lon_dev, kpad)

    where = packed[:, :, 0].astype(jnp.int32).reshape(-1, 1)
    weights = packed[:, :, 1:].reshape(-1, 4)
    position = jnp.arange(lat_dev * lon_dev, dtype=jnp.int32)[None, :]
    interp = None
    for corner, offset in enumerate((0, 1, lon_dev, lon_dev + 1)):
        term = jnp.where(position == where + offset, weights[:, corner, None], 0.0)
        interp = term if interp is None else interp + term
    profile = jnp.einsum(
        "rp,tpn->trn", interp, increment, precision=lax.Precision.HIGH,
        preferred_element_type=f32,
    ).astype(jnp.bfloat16)
    operator = jnp.pad(obs_operator, ((0, 0), (0, extra)))
    evolved = jnp.einsum(
        "trn,on->rto", profile, operator, preferred_element_type=f32
    ).reshape(devices_all, capacity, trials, channels)
    returned = lax.all_to_all(evolved, ("band", "sector"), 0, 0, tiled=True)

    observed = obs_values.reshape(devices_all, capacity, 1, channels)
    inverse = obs_inv_err.reshape(devices_all, capacity, 1, channels)
    live = counts[0][:, None] > jnp.arange(capacity, dtype=jnp.int32)[None, :]
    weighted = (returned - observed) * inverse
    departures = jnp.where(live[:, :, None, None], weighted, 0.0)
    misfit = jnp.sum(departures * departures, axis=(0, 1, 3))

    totals = xor_total(jnp.stack([background, misfit]), ("sector", "band"))
    cell_count = num_lines * lat_dev * lon_dev * devices_all
    cost_values = 0.5 * (totals[0] + totals[1]) / cell_count
    return (departures.reshape(devices_all * capacity, trials, channels), cost_values)


def solution(mesh):
    placed = (
        P(None, "band", "sector"),
        P(None, "band", "sector"),
        P(),
        P(),
        P(),
        P(),
        P(),
        P(("band", "sector"), None),
        P(("band", "sector"), None),
        P(("band", "sector")),
        P(("band", "sector"), None),
        P(("band", "sector"), None),
    )
    return jax.shard_map(
        body,
        mesh=mesh,
        in_specs=placed,
        out_specs=(P(("band", "sector"), None, None), P()),
        check_vma=False,
    )
```
